256 devices in a mesh: rows: 64 (over z, y, x_hi), cent: 4 (over x_lo, core).
Axes of the slice: x: 4 (x_hi: 2, x_lo: 2; x = x_hi * 2 + x_lo), y: 4, z: 8, core: 2. Of those that a mesh axis runs over, the one named last changes fastest.
Arguments:
- embeddings: bfloat16 [131072, 4096], P('rows', 'cent'), may hold values from -6 to 6
- basis: bfloat16 [4096, 512], P('cent'), may hold values from -0.09375 to 0.09375
- start_centroids: float32 [4096, 512], P('cent'), as said below
Outputs:
- centroids: float32 [4096, 512], P('cent')
- log_total: float32 [131072], P('rows')
The draws below stay inside these ranges and needn't reach their ends.
Inputs may be any that keep to these rules, and one draw needn't show every extreme that they name: `start_centroids`: initial centroids, real-valued; some may lie far from the others.
All inputs are finite; a program needn't handle non-finite values.
Results may differ from the reference program's by a relative error of at most 0.0024.
The reference program's roundings to bfloat16 on the way count: a program that leaves them out, or rounds other values in their place, can miss the bound.
Values may be sent and summed in bfloat16 or wider, within the bound.
No kernel may reach another device: no remote copies, remote signals or barrier semaphores. Data moves between devices by JAX's collectives and lax.ppermute only.
A program may use at most 64 MiB of HBM per device.

```python
import jax
import jax.numpy as jnp
from jax import lax

EMB = 4096
PROJ = 512
CLUSTERS = 4096
ITERS = 2
TOTAL_ROWS = 131072


def draw_start_centroids(key, part):
    base = jax.random.normal(jax.random.fold_in(key, 11), (CLUSTERS, PROJ), jnp.float32)
    offset = jax.random.randint(jax.random.fold_in(key, 13), (), 0, CLUSTERS)
    index = (jnp.arange(CLUSTERS) + offset) % CLUSTERS
    half = CLUSTERS // 2
    position = index % half
    which = index // half
    far = position < 2
    shared = jax.random.normal(jax.random.fold_in(key, 14), (2, PROJ), jnp.float32)
    strength = jnp.where(which == 0, 150.0, 60.0)
    unit = 8.0 / jnp.sqrt(jnp.float32(PROJ))
    apart = jax.random.normal(jax.random.fold_in(key, 15), (CLUSTERS, PROJ), jnp.float32)
    lead = shared[which] * (unit * strength)[:, None]
    second = jnp.where(position == 1, 1.0, 0.0)[:, None] * apart * (2.0 * unit)
    return jnp.where(far[:, None], lead + second, base)


def levels(key, extent, pieces, least, high):
    level = 1.0
    for dim, blocks in pieces:
        heights = jax.random.uniform(jax.random.fold_in(jax.random.fold_in(key, 6), dim), (blocks,), jnp.float32, least / len(pieces), high / len(pieces))
        level = level * jnp.repeat(jnp.exp(heights), extent[dim] // blocks).reshape((-1,) + (1,) * (len(extent) - 1 - dim))
    return level


def noise(stream_key, extent, spread, most, cuts=(), dtype=jnp.bfloat16):
    array = jax.random.normal(stream_key, extent, jnp.float32) * spread
    if len(cuts) > 0:
        array = levels(stream_key, extent, cuts, -0.22, 0.18) * array
    return jnp.clip(array, min=-most, max=most).astype(dtype)


def setup_inputs(seed: int = 0) -> dict:
    seeds = jax.random.split(jax.random.key(seed), 4)
    embeddings = noise(seeds[0], (TOTAL_ROWS, EMB), 1.0, 6.0, ((0, 64), (1, 4)))
    basis = noise(seeds[1], (EMB, PROJ), EMB ** -0.5, 0.09375, ((0, 4),))
    start_centroids = draw_start_centroids(jax.random.fold_in(seeds[3], 71), 0)
    return {"embeddings": embeddings, "basis": basis, "start_centroids": start_centroids}


TEMPER = 8.0


def reference(embeddings, basis, start_centroids):
    block = min(TOTAL_ROWS, 4096)
    count = TOTAL_ROWS // block
    emb_blocks = embeddings.reshape(count, block, EMB)
    projected = lax.map(lambda e: jnp.dot(e, basis, preferred_element_type=jnp.float32).astype(jnp.bfloat16), emb_blocks)
    centroids = start_centroids
    log_total = jnp.zeros((count, block), jnp.float32)
    for step in range(ITERS):
        cent_bf = centroids.astype(jnp.bfloat16)

        def one_block(carry, zrows):
            numer, mass = carry
            scores = jnp.dot(zrows, cent_bf.T, preferred_element_type=jnp.float32) / TEMPER
            top = jnp.max(scores, axis=1)
            lse = top + jnp.log(jnp.sum(jnp.exp(scores - top[:, None]), axis=1))
            weights = jnp.exp(scores - lse[:, None])
            mass = mass + jnp.sum(weights, axis=0)
            numer = numer + jnp.dot(weights.astype(jnp.bfloat16).T, zrows, preferred_element_type=jnp.float32)
            return (numer, mass), lse

        init = (jnp.zeros((CLUSTERS, PROJ), jnp.float32), jnp.zeros((CLUSTERS,), jnp.float32))
        (numer, mass), log_total = lax.scan(one_block, init, projected)
        centroids = (numer + centroids) / (mass[:, None] + 1.0)
    return centroids, log_total.reshape(TOTAL_ROWS)
```

```python
import jax
import jax.numpy as jnp
from jax import lax
from jax.sharding import Mesh
from jax.sharding import PartitionSpec as P

ITERS = 2


TEMPER = 8.0

ROW_AXES = ("z", "y", "xh")
CENT_AXES = ("xl", "core")


def _reduce_rows(numer, mass):
    count, width = numer.shape
    blocks = 8
    per = count // blocks
    mass_rows = jnp.zeros((blocks, 8, width), jnp.float32).at[:, 0, :per].set(mass.reshape(blocks, per))
    payload = jnp.concatenate([numer.reshape(blocks, per, width), mass_rows], axis=1)
    payload = payload.reshape(blocks * (per + 8), width)
    payload = lax.psum_scatter(payload, "z", scatter_dimension=0, tiled=True)
    payload = lax.psum(payload, "y")
    payload = lax.psum(payload, "xh")
    return payload[:per], payload[per, :per]


def _gather_rows(block):
    return lax.all_gather(block, "z", axis=0, tiled=True)


def _row_index():
    return lax.axis_index("z")


def on_device(embeddings, basis, start_centroids):
    row_count = embeddings.shape[0]
    count = start_centroids.shape[0]
    per = count // 8
    proj_share = lax.psum_scatter(
        jnp.dot(embeddings, basis, preferred_element_type=jnp.float32),
        CENT_AXES,
        scatter_dimension=0,
        tiled=True,
    )
    projected = lax.all_gather(proj_share.astype(jnp.bfloat16), CENT_AXES, axis=0, tiled=True)
    start = _row_index() * per
    block = lax.dynamic_slice_in_dim(start_centroids, start, per, axis=0)
    cent_bf = start_centroids.astype(jnp.bfloat16)
    log_total = jnp.zeros((row_count,), jnp.float32)
    for step in range(ITERS):
        scores = (
            lax.dot_general(
                projected, cent_bf, (((1,), (1,)), ((), ())), preferred_element_type=jnp.float32
            )
            / TEMPER
        )
        local_top = jnp.max(scores, axis=1)
        top = lax.pmax(local_top, CENT_AXES)
        total = lax.psum(jnp.sum(jnp.exp(scores - top[:, None]), axis=1), CENT_AXES)
        log_total = top + jnp.log(total)
        weights = jnp.exp(scores - log_total[:, None])
        local_mass = jnp.sum(weights, axis=0)
        local_numer = lax.dot_general(
            weights.astype(jnp.bfloat16),
            projected,
            (((0,), (0,)), ((), ())),
            preferred_element_type=jnp.float32,
        )
        numer, mass = _reduce_rows(local_numer, local_mass)
        block = (numer + block) / (mass[:, None] + 1.0)
        if step + 1 < ITERS:
            cent_bf = _gather_rows(block.astype(jnp.bfloat16))
    centroids = _gather_rows(block)
    return (centroids, log_total)


def solution(mesh):
    fine = Mesh(mesh.devices.reshape(8, 4, 2, 2, 2), ROW_AXES + CENT_AXES)
    return jax.shard_map(
        on_device,
        mesh=fine,
        in_specs=(P(ROW_AXES, CENT_AXES), P(CENT_AXES, None), P(CENT_AXES, None)),
        out_specs=(P(CENT_AXES, None), P(ROW_AXES)),
        check_vma=False,
    )
```

```python
import jax
import jax.numpy as jnp
from jax import lax
from jax.sharding import Mesh
from jax.sharding import PartitionSpec as P

ITERS = 2


TEMPER = 8.0

ROW_AXES = ("z", "y", "xh")
CENT_AXES = ("xl", "core")


def _reduce_rows(numer, mass):
    count, width = numer.shape
    mass_rows = jnp.zeros((8, width), jnp.float32).at[: count // width].set(mass.reshape(count // width, width))
    mine = jnp.concatenate([numer, mass_rows], axis=0)
    xl = lax.axis_index("xl")
    payload = jnp.stack([jnp.where(xl == slot, mine, 0.0) for slot in range(2)])
    payload = lax.psum(payload, ROW_AXES + ("xl",))
    total = lax.dynamic_index_in_dim(payload, xl, axis=0, keepdims=False)
    return total[:count], total[count : count + count // width].reshape(count)


def on_device(embeddings, basis, start_centroids):
    row_count = embeddings.shape[0]
    proj_share = lax.psum_scatter(
        jnp.dot(embeddings, basis, preferred_element_type=jnp.float32),
        CENT_AXES,
        scatter_dimension=0,
        tiled=True,
    )
    projected = lax.all_gather(proj_share.astype(jnp.bfloat16), CENT_AXES, axis=0, tiled=True)
    centroids = start_centroids
    cent_bf = start_centroids.astype(jnp.bfloat16)
    log_total = jnp.zeros((row_count,), jnp.float32)
    for step in range(ITERS):
        scores = (
            lax.dot_general(
                projected, cent_bf, (((1,), (1,)), ((), ())), preferred_element_type=jnp.float32
            )
            / TEMPER
        )
        local_top = jnp.max(scores, axis=1)
        top = lax.pmax(local_top, CENT_AXES)
        total = lax.psum(jnp.sum(jnp.exp(scores - top[:, None]), axis=1), CENT_AXES)
        log_total = top + jnp.log(total)
        weights = jnp.exp(scores - log_total[:, None])
        local_mass = jnp.sum(weights, axis=0)
        local_numer = lax.dot_general(
            weights.astype(jnp.bfloat16),
            projected,
            (((0,), (0,)), ((), ())),
            preferred_element_type=jnp.float32,
        )
        numer, mass = _reduce_rows(local_numer, local_mass)
        centroids = (numer + centroids) / (mass[:, None] + 1.0)
        cent_bf = centroids.astype(jnp.bfloat16)
    return (centroids, log_total)


def solution(mesh):
    fine = Mesh(mesh.devices.reshape(8, 4, 2, 2, 2), ROW_AXES + CENT_AXES)
    return jax.shard_map(
        on_device,
        mesh=fine,
        in_specs=(P(ROW_AXES, CENT_AXES), P(CENT_AXES, None), P(CENT_AXES, None)),
        out_specs=(P(CENT_AXES, None), P(ROW_AXES)),
        check_vma=False,
    )
```

```python
import jax
import jax.numpy as jnp
from jax import lax
from jax.sharding import Mesh
from jax.sharding import PartitionSpec as P

ITERS = 2


TEMPER = 8.0

ROW_AXES = ("z", "y", "xh")
CENT_AXES = ("xl", "core")


def _swap(x, axis, bit):
    size = {"y": 4, "xh": 2}[axis]
    return lax.ppermute(x, axis, [(i, i ^ bit) for i in range(size)])


def _bits():
    y = lax.axis_index("y")
    return ((y & 1, "y", 1), ((y >> 1) & 1, "y", 2), (lax.axis_index("xh"), "xh", 1))


def _reduce_rows(numer, mass):
    count, width = numer.shape
    blocks = 8
    per = count // blocks
    mass_rows = jnp.zeros((blocks, 8, width), jnp.float32).at[:, 0, :per].set(mass.reshape(blocks, per))
    payload = jnp.concatenate([numer.reshape(blocks, per, width), mass_rows], axis=1)
    payload = payload.reshape(blocks * (per + 8), width)
    payload = lax.psum_scatter(payload, "z", scatter_dimension=0, tiled=True)
    numer, mass = payload[:per], payload[per, :per]
    for bit, axis, mask in _bits():
        half = numer.shape[0] // 2
        keep = lax.dynamic_slice_in_dim(numer, bit * half, half, axis=0)
        send = lax.dynamic_slice_in_dim(numer, (1 - bit) * half, half, axis=0)
        keep_mass = lax.dynamic_slice_in_dim(mass, bit * half, half, axis=0)
        send_mass = lax.dynamic_slice_in_dim(mass, (1 - bit) * half, half, axis=0)
        numer = keep + _swap(send, axis, mask)
        mass = keep_mass + _swap(send_mass, axis, mask)
    return numer, mass


def _gather_rows(block):
    for bit, axis, mask in reversed(_bits()):
        other = _swap(block, axis, mask)
        block = jnp.where(bit == 0, jnp.concatenate([block, other]), jnp.concatenate([other, block]))
    return lax.all_gather(block, "z", axis=0, tiled=True)


def _row_offset(count):
    y = lax.axis_index("y")
    per = count // 64
    return lax.axis_index("z") * (count // 8) + (y & 1) * (4 * per) + ((y >> 1) & 1) * (2 * per) + lax.axis_index("xh") * per


def on_device(embeddings, basis, start_centroids):
    row_count = embeddings.shape[0]
    count = start_centroids.shape[0]
    per = count // 64
    proj_share = lax.psum_scatter(
        jnp.dot(embeddings, basis, preferred_element_type=jnp.float32),
        CENT_AXES,
        scatter_dimension=0,
        tiled=True,
    )
    projected = lax.all_gather(proj_share.astype(jnp.bfloat16), CENT_AXES, axis=0, tiled=True)
    start = _row_offset(count)
    block = lax.dynamic_slice_in_dim(start_centroids, start, per, axis=0)
    cent_bf = start_centroids.astype(jnp.bfloat16)
    log_total = jnp.zeros((row_count,), jnp.float32)
    for step in range(ITERS):
        scores = (
            lax.dot_general(
                projected, cent_bf, (((1,), (1,)), ((), ())), preferred_element_type=jnp.float32
            )
            / TEMPER
        )
        local_top = jnp.max(scores, axis=1)
        top = lax.pmax(local_top, CENT_AXES)
        total = lax.psum(jnp.sum(jnp.exp(scores - top[:, None]), axis=1), CENT_AXES)
        log_total = top + jnp.log(total)
        weights = jnp.exp(scores - log_total[:, None])
        local_mass = jnp.sum(weights, axis=0)
        local_numer = lax.dot_general(
            weights.astype(jnp.bfloat16),
            projected,
            (((0,), (0,)), ((), ())),
            preferred_element_type=jnp.float32,
        )
        numer, mass = _reduce_rows(local_numer, local_mass)
        block = (numer + block) / (mass[:, None] + 1.0)
        if step + 1 < ITERS:
            cent_bf = _gather_rows(block.astype(jnp.bfloat16))
    centroids = _gather_rows(block)
    return (centroids, log_total)


def solution(mesh):
    fine = Mesh(mesh.devices.reshape(8, 4, 2, 2, 2), ROW_AXES + CENT_AXES)
    return jax.shard_map(
        on_device,
        mesh=fine,
        in_specs=(P(ROW_AXES, CENT_AXES), P(CENT_AXES, None), P(CENT_AXES, None)),
        out_specs=(P(CENT_AXES, None), P(ROW_AXES)),
        check_vma=False,
    )
```

```python
import jax
import jax.numpy as jnp
from jax import lax
from jax.sharding import Mesh
from jax.sharding import PartitionSpec as P

ITERS = 2


TEMPER = 8.0

ROW_AXES = ("z", "y", "xh")
CENT_AXES = ("xl", "core")


def _swap(x, axis, bit):
    size = {"y": 4, "xh": 2}[axis]
    return lax.ppermute(x, axis, [(i, i ^ bit) for i in range(size)])


def _bits():
    y = lax.axis_index("y")
    return ((y & 1, "y", 1), ((y >> 1) & 1, "y", 2), (lax.axis_index("xh"), "xh", 1))


def _reduce_rows(numer, mass):
    count, width = numer.shape
    blocks = 8
    per = count // blocks
    mass_rows = jnp.zeros((blocks, 8, width), jnp.float32).at[:, 0, :per].set(mass.reshape(blocks, per))
    payload = jnp.concatenate([numer.reshape(blocks, per, width), mass_rows], axis=1)
    payload = payload.reshape(blocks * (per + 8), width)
    payload = lax.psum_scatter(payload, "z", scatter_dimension=0, tiled=True)
    numer, mass = payload[:per], payload[per, :per]
    for bit, axis, mask in _bits():
        half = numer.shape[0] // 2
        keep = lax.dynamic_slice_in_dim(numer, bit * half, half, axis=0)
        send = lax.dynamic_slice_in_dim(numer, (1 - bit) * half, half, axis=0)
        keep_mass = lax.dynamic_slice_in_dim(mass, bit * half, half, axis=0)
        send_mass = lax.dynamic_slice_in_dim(mass, (1 - bit) * half, half, axis=0)
        numer = keep + _swap(send, axis, mask)
        mass = keep_mass + _swap(send_mass, axis, mask)
    return numer, mass


def _gather_rows(block):
    for bit, axis, mask in reversed(_bits()):
        other = _swap(block, axis, mask)
        block = jnp.where(bit == 0, jnp.concatenate([block, other]), jnp.concatenate([other, block]))
    return lax.all_gather(block, "z", axis=0, tiled=True)


def _row_offset(count):
    y = lax.axis_index("y")
    per = count // 64
    return lax.axis_index("z") * (count // 8) + (y & 1) * (4 * per) + ((y >> 1) & 1) * (2 * per) + lax.axis_index("xh") * per


def _project(embeddings, basis):
    partial = jnp.dot(embeddings, basis, preferred_element_type=jnp.float32)
    steps = ((lax.axis_index("core"), "core"), (lax.axis_index("xl"), "xl"))
    for bit, axis in steps:
        half = partial.shape[0] // 2
        keep = lax.dynamic_slice_in_dim(partial, bit * half, half, axis=0)
        send = lax.dynamic_slice_in_dim(partial, (1 - bit) * half, half, axis=0)
        partial = keep + lax.ppermute(send, axis, [(0, 1), (1, 0)])
    block = partial.astype(jnp.bfloat16)
    for bit, axis in reversed(steps):
        other = lax.ppermute(block, axis, [(0, 1), (1, 0)])
        block = jnp.where(bit == 0, jnp.concatenate([block, other]), jnp.concatenate([other, block]))
    return block


def on_device(embeddings, basis, start_centroids):
    row_count = embeddings.shape[0]
    count = start_centroids.shape[0]
    per = count // 64
    projected = _project(embeddings, basis)
    start = _row_offset(count)
    block = lax.dynamic_slice_in_dim(start_centroids, start, per, axis=0)
    cent_bf = start_centroids.astype(jnp.bfloat16)
    log_total = jnp.zeros((row_count,), jnp.float32)
    for step in range(ITERS):
        scores = (
            lax.dot_general(
                projected, cent_bf, (((1,), (1,)), ((), ())), preferred_element_type=jnp.float32
            )
            / TEMPER
        )
        local_top = jnp.max(scores, axis=1)
        top = lax.pmax(local_top, CENT_AXES)
        total = lax.psum(jnp.sum(jnp.exp(scores - top[:, None]), axis=1), CENT_AXES)
        log_total = top + jnp.log(total)
        weights = jnp.exp(scores - log_total[:, None])
        local_mass = jnp.sum(weights, axis=0)
        local_numer = lax.dot_general(
            weights.astype(jnp.bfloat16),
            projected,
            (((0,), (0,)), ((), ())),
            preferred_element_type=jnp.float32,
        )
        numer, mass = _reduce_rows(local_numer, local_mass)
        block = (numer + block) / (mass[:, None] + 1.0)
        if step + 1 < ITERS:
            cent_bf = _gather_rows(block.astype(jnp.bfloat16))
    centroids = _gather_rows(block)
    return (centroids, log_total)


def solution(mesh):
    fine = Mesh(mesh.devices.reshape(8, 4, 2, 2, 2), ROW_AXES + CENT_AXES)
    return jax.shard_map(
        on_device,
        mesh=fine,
        in_specs=(P(ROW_AXES, CENT_AXES), P(CENT_AXES, None), P(CENT_AXES, None)),
        out_specs=(P(CENT_AXES, None), P(ROW_AXES)),
        check_vma=False,
    )
```

```python
import jax
import jax.numpy as jnp
from jax import lax
from jax.sharding import Mesh
from jax.sharding import PartitionSpec as P

ITERS = 2


TEMPER = 8.0

ROW_AXES = ("z", "y", "xh")
CENT_AXES = ("xl", "core")


def _swap(x, axis, bit):
    size = {"y": 4, "xh": 2}[axis]
    return lax.ppermute(x, axis, [(i, i ^ bit) for i in range(size)])


def _bits():
    y = lax.axis_index("y")
    return ((y & 1, "y", 1), ((y >> 1) & 1, "y", 2), (lax.axis_index("xh"), "xh", 1))


def _reduce_rows(numer, mass):
    count, width = numer.shape
    blocks = 8
    per = count // blocks
    mass_rows = jnp.zeros((blocks, 8, width), jnp.float32).at[:, 0, :per].set(mass.reshape(blocks, per))
    payload = jnp.concatenate([numer.reshape(blocks, per, width), mass_rows], axis=1)
    payload = payload.reshape(blocks * (per + 8), width)
    payload = lax.psum_scatter(payload, "z", scatter_dimension=0, tiled=True)
    numer, mass = payload[:per], payload[per, :per]
    for bit, axis, mask in _bits():
        half = numer.shape[0] // 2
        keep = lax.dynamic_slice_in_dim(numer, bit * half, half, axis=0)
        send = lax.dynamic_slice_in_dim(numer, (1 - bit) * half, half, axis=0)
        keep_mass = lax.dynamic_slice_in_dim(mass, bit * half, half, axis=0)
        send_mass = lax.dynamic_slice_in_dim(mass, (1 - bit) * half, half, axis=0)
        numer = keep + _swap(send, axis, mask)
        mass = keep_mass + _swap(send_mass, axis, mask)
    return numer, mass


def _gather_rows(block):
    for bit, axis, mask in reversed(_bits()):
        other = _swap(block, axis, mask)
        block = jnp.where(bit == 0, jnp.concatenate([block, other]), jnp.concatenate([other, block]))
    return _ring_gather_z(block)


def _ring_gather_z(block):
    n = 8
    rows = block.shape[0]
    up = [(i, (i + 1) % n) for i in range(n)]
    down = [(i, (i - 1) % n) for i in range(n)]
    cw, ccw = block, block
    before, after = [], []
    for k in range(1, n // 2 + 1):
        cw = lax.ppermute(cw, "z", up)
        before.append(cw)
        if k < n // 2:
            ccw = lax.ppermute(ccw, "z", down)
            after.append(ccw)
    stacked = jnp.concatenate(list(reversed(before)) + [block] + after, axis=0)
    doubled = jnp.concatenate([stacked, stacked], axis=0)
    shift = (n // 2 - lax.axis_index("z")) % n
    return lax.dynamic_slice_in_dim(doubled, shift * rows, n * rows, axis=0)


def _row_offset(count):
    y = lax.axis_index("y")
    per = count // 64
    return lax.axis_index("z") * (count // 8) + (y & 1) * (4 * per) + ((y >> 1) & 1) * (2 * per) + lax.axis_index("xh") * per


def _project(embeddings, basis):
    partial = jnp.dot(embeddings, basis, preferred_element_type=jnp.float32)
    steps = ((lax.axis_index("core"), "core"), (lax.axis_index("xl"), "xl"))
    for bit, axis in steps:
        half = partial.shape[0] // 2
        keep = lax.dynamic_slice_in_dim(partial, bit * half, half, axis=0)
        send = lax.dynamic_slice_in_dim(partial, (1 - bit) * half, half, axis=0)
        partial = keep + lax.ppermute(send, axis, [(0, 1), (1, 0)])
    block = partial.astype(jnp.bfloat16)
    for bit, axis in reversed(steps):
        other = lax.ppermute(block, axis, [(0, 1), (1, 0)])
        block = jnp.where(bit == 0, jnp.concatenate([block, other]), jnp.concatenate([other, block]))
    return block


def on_device(embeddings, basis, start_centroids):
    row_count = embeddings.shape[0]
    count = start_centroids.shape[0]
    per = count // 64
    projected = _project(embeddings, basis)
    start = _row_offset(count)
    block = lax.dynamic_slice_in_dim(start_centroids, start, per, axis=0)
    log_total = jnp.zeros((row_count,), jnp.float32)

    def one_step(_, carry):
        block, centroids, log_total = carry
        cent_bf = centroids.astype(jnp.bfloat16)
        scores = (
            lax.dot_general(
                projected, cent_bf, (((1,), (1,)), ((), ())), preferred_element_type=jnp.float32
            )
            / TEMPER
        )
        local_top = jnp.max(scores, axis=1)
        top = lax.pmax(local_top, CENT_AXES)
        total = lax.psum(jnp.sum(jnp.exp(scores - top[:, None]), axis=1), CENT_AXES)
        log_total = top + jnp.log(total)
        weights = jnp.exp(scores - log_total[:, None])
        local_mass = jnp.sum(weights, axis=0)
        local_numer = lax.dot_general(
            weights.astype(jnp.bfloat16),
            projected,
            (((0,), (0,)), ((), ())),
            preferred_element_type=jnp.float32,
        )
        numer, mass = _reduce_rows(local_numer, local_mass)
        block = (numer + block) / (mass[:, None] + 1.0)
        return block, _gather_rows(block), log_total

    _, centroids, log_total = lax.fori_loop(0, ITERS, one_step, (block, start_centroids, log_total))
    return (centroids, log_total)


def solution(mesh):
    fine = Mesh(mesh.devices.reshape(8, 4, 2, 2, 2), ROW_AXES + CENT_AXES)
    return jax.shard_map(
        on_device,
        mesh=fine,
        in_specs=(P(ROW_AXES, CENT_AXES), P(CENT_AXES, None), P(CENT_AXES, None)),
        out_specs=(P(CENT_AXES, None), P(ROW_AXES)),
        check_vma=False,
    )
```

```python
import jax
import jax.numpy as jnp
from jax import lax
from jax.sharding import Mesh
from jax.sharding import PartitionSpec as P

ITERS = 2


TEMPER = 8.0

ROW_AXES = ("z", "y", "xh")
CENT_AXES = ("xl", "core")


GROUP = ("y", "xh")
GROUP_SIZE = 8


def _shift(x, s):
    return lax.ppermute(x, GROUP, [(i, (i + s) % GROUP_SIZE) for i in range(GROUP_SIZE)])


def _group_index():
    return lax.axis_index("y") * 2 + lax.axis_index("xh")


def _reduce_rows(numer, mass):
    count, width = numer.shape
    blocks = 8
    per = count // blocks
    mass_rows = jnp.zeros((blocks, 8, width), jnp.float32).at[:, 0, :per].set(mass.reshape(blocks, per))
    payload = jnp.concatenate([numer.reshape(blocks, per, width), mass_rows], axis=1)
    payload = payload.reshape(blocks * (per + 8), width)
    payload = lax.psum_scatter(payload, "z", scatter_dimension=0, tiled=True)
    numer, mass = payload[:per], payload[per, :per]
    chunk = per // GROUP_SIZE
    mass_row = jnp.zeros((GROUP_SIZE, 1, width), jnp.float32).at[:, 0, :chunk].set(mass.reshape(GROUP_SIZE, chunk))
    chunks = jnp.concatenate([numer.reshape(GROUP_SIZE, chunk, width), mass_row], axis=1)
    g = _group_index()
    total = lax.dynamic_index_in_dim(chunks, g, axis=0, keepdims=False)
    for s in range(1, GROUP_SIZE):
        total = total + _shift(lax.dynamic_index_in_dim(chunks, (g + s) % GROUP_SIZE, axis=0, keepdims=False), s)
    return total[:chunk], total[chunk, :chunk]


def _gather_rows(block):
    g = _group_index()
    got = [block] + [_shift(block, s) for s in range(1, GROUP_SIZE)]
    stacked = jnp.concatenate(list(reversed(got)), axis=0)
    doubled = jnp.concatenate([stacked, stacked], axis=0)
    rows = block.shape[0]
    start = (GROUP_SIZE - 1 - g) % GROUP_SIZE
    group_block = lax.dynamic_slice_in_dim(doubled, start * rows, GROUP_SIZE * rows, axis=0)
    return lax.all_gather(group_block, "z", axis=0, tiled=True)


def _row_offset(count):
    return lax.axis_index("z") * (count // 8) + _group_index() * (count // 64)


def _project(embeddings, basis):
    partial = jnp.dot(embeddings, basis, preferred_element_type=jnp.float32)
    steps = ((lax.axis_index("core"), "core"), (lax.axis_index("xl"), "xl"))
    for bit, axis in steps:
        half = partial.shape[0] // 2
        keep = lax.dynamic_slice_in_dim(partial, bit * half, half, axis=0)
        send = lax.dynamic_slice_in_dim(partial, (1 - bit) * half, half, axis=0)
        partial = keep + lax.ppermute(send, axis, [(0, 1), (1, 0)])
    block = partial.astype(jnp.bfloat16)
    for bit, axis in reversed(steps):
        other = lax.ppermute(block, axis, [(0, 1), (1, 0)])
        block = jnp.where(bit == 0, jnp.concatenate([block, other]), jnp.concatenate([other, block]))
    return block


def on_device(embeddings, basis, start_centroids):
    row_count = embeddings.shape[0]
    count = start_centroids.shape[0]
    per = count // 64
    projected = _project(embeddings, basis)
    start = _row_offset(count)
    block = lax.dynamic_slice_in_dim(start_centroids, start, per, axis=0)
    cent_bf = start_centroids.astype(jnp.bfloat16)
    log_total = jnp.zeros((row_count,), jnp.float32)
    for step in range(ITERS):
        scores = (
            lax.dot_general(
                projected, cent_bf, (((1,), (1,)), ((), ())), preferred_element_type=jnp.float32
            )
            / TEMPER
        )
        local_top = jnp.max(scores, axis=1)
        top = lax.pmax(local_top, CENT_AXES)
        total = lax.psum(jnp.sum(jnp.exp(scores - top[:, None]), axis=1), CENT_AXES)
        log_total = top + jnp.log(total)
        weights = jnp.exp(scores - log_total[:, None])
        local_mass = jnp.sum(weights, axis=0)
        local_numer = lax.dot_general(
            weights.astype(jnp.bfloat16),
            projected,
            (((0,), (0,)), ((), ())),
            preferred_element_type=jnp.float32,
        )
        numer, mass = _reduce_rows(local_numer, local_mass)
        block = (numer + block) / (mass[:, None] + 1.0)
        if step + 1 < ITERS:
            cent_bf = _gather_rows(block.astype(jnp.bfloat16))
    centroids = _gather_rows(block)
    return (centroids, log_total)


def solution(mesh):
    fine = Mesh(mesh.devices.reshape(8, 4, 2, 2, 2), ROW_AXES + CENT_AXES)
    return jax.shard_map(
        on_device,
        mesh=fine,
        in_specs=(P(ROW_AXES, CENT_AXES), P(CENT_AXES, None), P(CENT_AXES, None)),
        out_specs=(P(CENT_AXES, None), P(ROW_AXES)),
        check_vma=False,
    )
```

```python
import jax
import jax.numpy as jnp
from jax import lax
from jax.sharding import Mesh
from jax.sharding import PartitionSpec as P

ITERS = 2


TEMPER = 8.0

ROW_AXES = ("z", "y", "xh")
CENT_AXES = ("xl", "core")


def _swap(x, axis, bit):
    size = {"y": 4, "xh": 2}[axis]
    return lax.ppermute(x, axis, [(i, i ^ bit) for i in range(size)])


def _bits():
    y = lax.axis_index("y")
    return ((y & 1, "y", 1), ((y >> 1) & 1, "y", 2), (lax.axis_index("xh"), "xh", 1))


def _reduce_rows(numer, mass):
    count, width = numer.shape
    blocks = 8
    per = count // blocks
    mass_rows = jnp.zeros((blocks, 8, width), jnp.float32).at[:, 0, :per].set(mass.reshape(blocks, per))
    payload = jnp.concatenate([numer.reshape(blocks, per, width), mass_rows], axis=1)
    payload = payload.reshape(blocks * (per + 8), width)
    payload = lax.psum_scatter(payload, "z", scatter_dimension=0, tiled=True)
    numer, mass = payload[:per], payload[per, :per]
    for bit, axis, mask in _bits():
        half = numer.shape[0] // 2
        keep = lax.dynamic_slice_in_dim(numer, bit * half, half, axis=0)
        send = lax.dynamic_slice_in_dim(numer, (1 - bit) * half, half, axis=0)
        keep_mass = lax.dynamic_slice_in_dim(mass, bit * half, half, axis=0)
        send_mass = lax.dynamic_slice_in_dim(mass, (1 - bit) * half, half, axis=0)
        numer = keep + _swap(send, axis, mask)
        mass = keep_mass + _swap(send_mass, axis, mask)
    return numer, mass


def _gather_rows(block):
    for bit, axis, mask in reversed(_bits()):
        other = _swap(block, axis, mask)
        block = jnp.where(bit == 0, jnp.concatenate([block, other]), jnp.concatenate([other, block]))
    return lax.all_gather(block, "z", axis=0, tiled=True)


def _row_offset(count):
    y = lax.axis_index("y")
    per = count // 64
    return lax.axis_index("z") * (count // 8) + (y & 1) * (4 * per) + ((y >> 1) & 1) * (2 * per) + lax.axis_index("xh") * per


def _project(embeddings, basis):
    partial = jnp.dot(embeddings, basis, preferred_element_type=jnp.float32)
    steps = ((lax.axis_index("core"), "core"), (lax.axis_index("xl"), "xl"))
    for bit, axis in steps:
        half = partial.shape[0] // 2
        keep = lax.dynamic_slice_in_dim(partial, bit * half, half, axis=0)
        send = lax.dynamic_slice_in_dim(partial, (1 - bit) * half, half, axis=0)
        partial = keep + lax.ppermute(send, axis, [(0, 1), (1, 0)])
    block = partial.astype(jnp.bfloat16)
    for bit, axis in reversed(steps):
        other = lax.ppermute(block, axis, [(0, 1), (1, 0)])
        block = jnp.where(bit == 0, jnp.concatenate([block, other]), jnp.concatenate([other, block]))
    return block


def _merge(a, b):
    top = jnp.maximum(a[0], b[0])
    return jnp.stack([top, a[1] * jnp.exp(a[0] - top) + b[1] * jnp.exp(b[0] - top)])


def _log_total(scores):
    local_top = jnp.max(scores, axis=1)
    pair = jnp.stack([local_top, jnp.sum(jnp.exp(scores - local_top[:, None]), axis=1)])
    for axis in ("core", "xl"):
        other = lax.ppermute(pair, axis, [(0, 1), (1, 0)])
        low = lax.axis_index(axis) == 0
        pair = _merge(jnp.where(low, pair, other), jnp.where(low, other, pair))
    return pair[0] + jnp.log(pair[1])


def on_device(embeddings, basis, start_centroids):
    row_count = embeddings.shape[0]
    count = start_centroids.shape[0]
    per = count // 64
    projected = _project(embeddings, basis)
    start = _row_offset(count)
    block = lax.dynamic_slice_in_dim(start_centroids, start, per, axis=0)
    cent_bf = start_centroids.astype(jnp.bfloat16)
    log_total = jnp.zeros((row_count,), jnp.float32)
    for step in range(ITERS):
        scores = (
            lax.dot_general(
                projected, cent_bf, (((1,), (1,)), ((), ())), preferred_element_type=jnp.float32
            )
            / TEMPER
        )
        log_total = _log_total(scores)
        weights = jnp.exp(scores - log_total[:, None])
        local_mass = jnp.sum(weights, axis=0)
        local_numer = lax.dot_general(
            weights.astype(jnp.bfloat16),
            projected,
            (((0,), (0,)), ((), ())),
            preferred_element_type=jnp.float32,
        )
        numer, mass = _reduce_rows(local_numer, local_mass)
        block = (numer + block) / (mass[:, None] + 1.0)
        if step + 1 < ITERS:
            cent_bf = _gather_rows(block.astype(jnp.bfloat16))
    centroids = _gather_rows(block)
    return (centroids, log_total)


def solution(mesh):
    fine = Mesh(mesh.devices.reshape(8, 4, 2, 2, 2), ROW_AXES + CENT_AXES)
    return jax.shard_map(
        on_device,
        mesh=fine,
        in_specs=(P(ROW_AXES, CENT_AXES), P(CENT_AXES, None), P(CENT_AXES, None)),
        out_specs=(P(CENT_AXES, None), P(ROW_AXES)),
        check_vma=False,
    )
```

```python
import jax
import jax.numpy as jnp
from jax import lax
from jax.sharding import Mesh
from jax.sharding import PartitionSpec as P

ITERS = 2


TEMPER = 8.0

ROW_AXES = ("z", "y", "xh")
CENT_AXES = ("xl", "core")


def _swap(x, axis, bit):
    size = {"y": 4, "xh": 2}[axis]
    return lax.ppermute(x, axis, [(i, i ^ bit) for i in range(size)])


def _bits():
    y = lax.axis_index("y")
    return ((y & 1, "y", 1), ((y >> 1) & 1, "y", 2), (lax.axis_index("xh"), "xh", 1))


def _reduce_rows(numer, mass):
    count, width = numer.shape
    blocks = 8
    per = count // blocks
    subs = 8
    sub = per // subs
    mass_rows = jnp.zeros((blocks, subs, width), jnp.float32).at[:, :, :sub].set(mass.reshape(blocks, subs, sub))
    payload = jnp.concatenate([numer.reshape(blocks, per, width), mass_rows], axis=1)
    payload = payload.reshape(blocks * (per + subs), width)
    state = lax.psum_scatter(payload, "z", scatter_dimension=0, tiled=True)
    rows, extra = per, subs
    for bit, axis, mask in _bits():
        rows, extra = rows // 2, extra // 2
        numer_part, mass_part = state[: 2 * rows], state[2 * rows :]

        def half(which):
            return jnp.concatenate(
                [
                    lax.dynamic_slice_in_dim(numer_part, which * rows, rows, axis=0),
                    lax.dynamic_slice_in_dim(mass_part, which * extra, extra, axis=0),
                ]
            )

        state = half(bit) + _swap(half(1 - bit), axis, mask)
    return state[:rows], state[rows, :rows]


def _gather_rows(block):
    for bit, axis, mask in reversed(_bits()):
        other = _swap(block, axis, mask)
        block = jnp.where(bit == 0, jnp.concatenate([block, other]), jnp.concatenate([other, block]))
    return lax.all_gather(block, "z", axis=0, tiled=True)


def _row_offset(count):
    y = lax.axis_index("y")
    per = count // 64
    return lax.axis_index("z") * (count // 8) + (y & 1) * (4 * per) + ((y >> 1) & 1) * (2 * per) + lax.axis_index("xh") * per


def _project(embeddings, basis):
    partial = jnp.dot(embeddings, basis, preferred_element_type=jnp.float32)
    steps = ((lax.axis_index("core"), "core"), (lax.axis_index("xl"), "xl"))
    for bit, axis in steps:
        half = partial.shape[0] // 2
        keep = lax.dynamic_slice_in_dim(partial, bit * half, half, axis=0)
        send = lax.dynamic_slice_in_dim(partial, (1 - bit) * half, half, axis=0)
        partial = keep + lax.ppermute(send, axis, [(0, 1), (1, 0)])
    block = partial.astype(jnp.bfloat16)
    for bit, axis in reversed(steps):
        other = lax.ppermute(block, axis, [(0, 1), (1, 0)])
        block = jnp.where(bit == 0, jnp.concatenate([block, other]), jnp.concatenate([other, block]))
    return block


def _merge(a, b):
    top = jnp.maximum(a[0], b[0])
    return jnp.stack([top, a[1] * jnp.exp(a[0] - top) + b[1] * jnp.exp(b[0] - top)])


def _log_total(scores):
    local_top = jnp.max(scores, axis=1)
    pair = jnp.stack([local_top, jnp.sum(jnp.exp(scores - local_top[:, None]), axis=1)])
    for axis in ("core", "xl"):
        other = lax.ppermute(pair, axis, [(0, 1), (1, 0)])
        low = lax.axis_index(axis) == 0
        pair = _merge(jnp.where(low, pair, other), jnp.where(low, other, pair))
    return pair[0] + jnp.log(pair[1])


def on_device(embeddings, basis, start_centroids):
    row_count = embeddings.shape[0]
    count = start_centroids.shape[0]
    per = count // 64
    projected = _project(embeddings, basis)
    start = _row_offset(count)
    block = lax.dynamic_slice_in_dim(start_centroids, start, per, axis=0)
    cent_bf = start_centroids.astype(jnp.bfloat16)
    log_total = jnp.zeros((row_count,), jnp.float32)
    for step in range(ITERS):
        scores = (
            lax.dot_general(
                projected, cent_bf, (((1,), (1,)), ((), ())), preferred_element_type=jnp.float32
            )
            / TEMPER
        )
        log_total = _log_total(scores)
        weights = jnp.exp(scores - log_total[:, None])
        local_mass = jnp.sum(weights, axis=0)
        local_numer = lax.dot_general(
            weights.astype(jnp.bfloat16),
            projected,
            (((0,), (0,)), ((), ())),
            preferred_element_type=jnp.float32,
        )
        numer, mass = _reduce_rows(local_numer, local_mass)
        block = (numer + block) / (mass[:, None] + 1.0)
        if step + 1 < ITERS:
            cent_bf = _gather_rows(block.astype(jnp.bfloat16))
    centroids = _gather_rows(block)
    return (centroids, log_total)


def solution(mesh):
    fine = Mesh(mesh.devices.reshape(8, 4, 2, 2, 2), ROW_AXES + CENT_AXES)
    return jax.shard_map(
        on_device,
        mesh=fine,
        in_specs=(P(ROW_AXES, CENT_AXES), P(CENT_AXES, None), P(CENT_AXES, None)),
        out_specs=(P(CENT_AXES, None), P(ROW_AXES)),
        check_vma=False,
    )
```

```python
import jax
import jax.numpy as jnp
from jax import lax
from jax.sharding import Mesh
from jax.sharding import PartitionSpec as P

ITERS = 2


TEMPER = 8.0

ROW_AXES = ("z", "y", "xh")
CENT_AXES = ("xl", "core")


def _swap(x, axis, bit):
    size = {"y": 4, "xh": 2}[axis]
    return lax.ppermute(x, axis, [(i, i ^ bit) for i in range(size)])


def _bits():
    y = lax.axis_index("y")
    return (((y >> 1) & 1, "y", 2), (y & 1, "y", 1), (lax.axis_index("xh"), "xh", 1))


def _reduce_rows(numer, mass):
    count, width = numer.shape
    blocks = 8
    per = count // blocks
    mass_rows = jnp.zeros((blocks, 8, width), jnp.float32).at[:, 0, :per].set(mass.reshape(blocks, per))
    payload = jnp.concatenate([numer.reshape(blocks, per, width), mass_rows], axis=1)
    payload = payload.reshape(blocks * (per + 8), width)
    payload = lax.psum_scatter(payload, "z", scatter_dimension=0, tiled=True)
    numer, mass = payload[:per], payload[per, :per]
    for bit, axis, mask in _bits():
        half = numer.shape[0] // 2
        keep = lax.dynamic_slice_in_dim(numer, bit * half, half, axis=0)
        send = lax.dynamic_slice_in_dim(numer, (1 - bit) * half, half, axis=0)
        keep_mass = lax.dynamic_slice_in_dim(mass, bit * half, half, axis=0)
        send_mass = lax.dynamic_slice_in_dim(mass, (1 - bit) * half, half, axis=0)
        numer = keep + _swap(send, axis, mask)
        mass = keep_mass + _swap(send_mass, axis, mask)
    return numer, mass


def _gather_rows(block):
    bit, axis, mask = _bits()[-1]
    other = _swap(block, axis, mask)
    block = jnp.where(bit == 0, jnp.concatenate([block, other]), jnp.concatenate([other, block]))
    return lax.all_gather(block, ("z", "y"), axis=0, tiled=True)


def _row_offset(count):
    per = count // 64
    return (lax.axis_index("z") * 4 + lax.axis_index("y")) * (2 * per) + lax.axis_index("xh") * per


def _project(embeddings, basis):
    partial = jnp.dot(embeddings, basis, preferred_element_type=jnp.float32)
    steps = ((lax.axis_index("core"), "core"), (lax.axis_index("xl"), "xl"))
    for bit, axis in steps:
        half = partial.shape[0] // 2
        keep = lax.dynamic_slice_in_dim(partial, bit * half, half, axis=0)
        send = lax.dynamic_slice_in_dim(partial, (1 - bit) * half, half, axis=0)
        partial = keep + lax.ppermute(send, axis, [(0, 1), (1, 0)])
    block = partial.astype(jnp.bfloat16)
    for bit, axis in reversed(steps):
        other = lax.ppermute(block, axis, [(0, 1), (1, 0)])
        block = jnp.where(bit == 0, jnp.concatenate([block, other]), jnp.concatenate([other, block]))
    return block


def _merge(a, b):
    top = jnp.maximum(a[0], b[0])
    return jnp.stack([top, a[1] * jnp.exp(a[0] - top) + b[1] * jnp.exp(b[0] - top)])


def _log_total(scores):
    local_top = jnp.max(scores, axis=1)
    pair = jnp.stack([local_top, jnp.sum(jnp.exp(scores - local_top[:, None]), axis=1)])
    for axis in ("core", "xl"):
        other = lax.ppermute(pair, axis, [(0, 1), (1, 0)])
        low = lax.axis_index(axis) == 0
        pair = _merge(jnp.where(low, pair, other), jnp.where(low, other, pair))
    return pair[0] + jnp.log(pair[1])


def on_device(embeddings, basis, start_centroids):
    row_count = embeddings.shape[0]
    count = start_centroids.shape[0]
    per = count // 64
    projected = _project(embeddings, basis)
    start = _row_offset(count)
    block = lax.dynamic_slice_in_dim(start_centroids, start, per, axis=0)
    cent_bf = start_centroids.astype(jnp.bfloat16)
    log_total = jnp.zeros((row_count,), jnp.float32)
    for step in range(ITERS):
        scores = (
            lax.dot_general(
                projected, cent_bf, (((1,), (1,)), ((), ())), preferred_element_type=jnp.float32
            )
            / TEMPER
        )
        log_total = _log_total(scores)
        weights = jnp.exp(scores - log_total[:, None])
        local_mass = jnp.sum(weights, axis=0)
        local_numer = lax.dot_general(
            weights.astype(jnp.bfloat16),
            projected,
            (((0,), (0,)), ((), ())),
            preferred_element_type=jnp.float32,
        )
        numer, mass = _reduce_rows(local_numer, local_mass)
        block = (numer + block) / (mass[:, None] + 1.0)
        if step + 1 < ITERS:
            cent_bf = _gather_rows(block.astype(jnp.bfloat16))
    centroids = _gather_rows(block)
    return (centroids, log_total)


def solution(mesh):
    fine = Mesh(mesh.devices.reshape(8, 4, 2, 2, 2), ROW_AXES + CENT_AXES)
    return jax.shard_map(
        on_device,
        mesh=fine,
        in_specs=(P(ROW_AXES, CENT_AXES), P(CENT_AXES, None), P(CENT_AXES, None)),
        out_specs=(P(CENT_AXES, None), P(ROW_AXES)),
        check_vma=False,
    )
```

```python
import jax
import jax.numpy as jnp
from jax import lax
from jax.sharding import Mesh
from jax.sharding import PartitionSpec as P

ITERS = 2


TEMPER = 8.0

ROW_AXES = ("z", "y", "xh")
CENT_AXES = ("xl", "core")


def _swap(x, axis, bit):
    size = {"y": 4, "xh": 2}[axis]
    return lax.ppermute(x, axis, [(i, i ^ bit) for i in range(size)])


def _bits():
    y = lax.axis_index("y")
    return ((y & 1, "y", 1), ((y >> 1) & 1, "y", 2), (lax.axis_index("xh"), "xh", 1))


def _reduce_rows(numer, mass):
    count, width = numer.shape
    blocks = 8
    per = count // blocks
    mass_rows = jnp.zeros((blocks, 8, width), jnp.float32).at[:, 0, :per].set(mass.reshape(blocks, per))
    payload = jnp.concatenate([numer.reshape(blocks, per, width), mass_rows], axis=1)
    payload = payload.reshape(blocks * (per + 8), width)
    payload = lax.psum_scatter(payload, "z", scatter_dimension=0, tiled=True)
    numer, mass = payload[:per], payload[per, :per]
    for bit, axis, mask in _bits():
        half = numer.shape[0] // 2
        keep = lax.dynamic_slice_in_dim(numer, bit * half, half, axis=0)
        send = lax.dynamic_slice_in_dim(numer, (1 - bit) * half, half, axis=0)
        keep_mass = lax.dynamic_slice_in_dim(mass, bit * half, half, axis=0)
        send_mass = lax.dynamic_slice_in_dim(mass, (1 - bit) * half, half, axis=0)
        numer = keep + _swap(send, axis, mask)
        mass = keep_mass + _swap(send_mass, axis, mask)
    return numer, mass


def _gather_rows(block):
    for bit, axis, mask in reversed(_bits()):
        other = _swap(block, axis, mask)
        block = jnp.where(bit == 0, jnp.concatenate([block, other]), jnp.concatenate([other, block]))
    return lax.all_gather(block, "z", axis=0, tiled=True)


def _row_offset(count):
    y = lax.axis_index("y")
    per = count // 64
    return lax.axis_index("z") * (count // 8) + (y & 1) * (4 * per) + ((y >> 1) & 1) * (2 * per) + lax.axis_index("xh") * per


def _project(embeddings, basis):
    partial = jnp.dot(embeddings, basis, preferred_element_type=jnp.float32)
    steps = ((lax.axis_index("core"), "core"), (lax.axis_index("xl"), "xl"))
    for bit, axis in steps:
        half = partial.shape[0] // 2
        keep = lax.dynamic_slice_in_dim(partial, bit * half, half, axis=0)
        send = lax.dynamic_slice_in_dim(partial, (1 - bit) * half, half, axis=0)
        partial = keep + lax.ppermute(send, axis, [(0, 1), (1, 0)])
    block = partial.astype(jnp.bfloat16)
    for bit, axis in reversed(steps):
        other = lax.ppermute(block, axis, [(0, 1), (1, 0)])
        block = jnp.where(bit == 0, jnp.concatenate([block, other]), jnp.concatenate([other, block]))
    return block


def _merge(a, b):
    top = jnp.maximum(a[0], b[0])
    return jnp.stack([top, a[1] * jnp.exp(a[0] - top) + b[1] * jnp.exp(b[0] - top)])


def _log_total(scores):
    local_top = jnp.max(scores, axis=1)
    pair = jnp.stack([local_top, jnp.sum(jnp.exp(scores - local_top[:, None]), axis=1)])
    for axis in ("core", "xl"):
        other = lax.ppermute(pair, axis, [(0, 1), (1, 0)])
        low = lax.axis_index(axis) == 0
        pair = _merge(jnp.where(low, pair, other), jnp.where(low, other, pair))
    return pair[0] + jnp.log(pair[1])


def on_device(embeddings, basis, start_centroids):
    row_count = embeddings.shape[0]
    count = start_centroids.shape[0]
    per = count // 64
    projected = _project(embeddings, basis)
    start = _row_offset(count)
    block = lax.dynamic_slice_in_dim(start_centroids, start, per, axis=0)
    log_total = jnp.zeros((row_count,), jnp.float32)

    def one_step(_, carry):
        block, centroids, log_total = carry
        cent_bf = centroids.astype(jnp.bfloat16)
        scores = (
            lax.dot_general(
                projected, cent_bf, (((1,), (1,)), ((), ())), preferred_element_type=jnp.float32
            )
            / TEMPER
        )
        log_total = _log_total(scores)
        weights = jnp.exp(scores - log_total[:, None])
        local_mass = jnp.sum(weights, axis=0)
        local_numer = lax.dot_general(
            weights.astype(jnp.bfloat16),
            projected,
            (((0,), (0,)), ((), ())),
            preferred_element_type=jnp.float32,
        )
        numer, mass = _reduce_rows(local_numer, local_mass)
        block = (numer + block) / (mass[:, None] + 1.0)
        return block, _gather_rows(block), log_total

    _, centroids, log_total = lax.fori_loop(0, ITERS, one_step, (block, start_centroids, log_total))
    return (centroids, log_total)


def solution(mesh):
    fine = Mesh(mesh.devices.reshape(8, 4, 2, 2, 2), ROW_AXES + CENT_AXES)
    return jax.shard_map(
        on_device,
        mesh=fine,
        in_specs=(P(ROW_AXES, CENT_AXES), P(CENT_AXES, None), P(CENT_AXES, None)),
        out_specs=(P(CENT_AXES, None), P(ROW_AXES)),
        check_vma=False,
    )
```
